1024 devices in a mesh: rows: 64 (over x, y), chip: 16 (over z, core).
Axes of the slice: x: 8, y: 8, z: 8, core: 2. Of those that a mesh axis runs over, the one named last changes fastest.
Arguments:
- spectra: float32 [262144, 512], P(('rows', 'chip')), may hold values from -250 to 250
Outputs:
- whitened: float32 [262144, 512], P(('rows', 'chip'))
- triangle: float32 [512, 512], replicated
The draws below stay inside these ranges and needn't reach their ends.
All inputs are finite; a program needn't handle non-finite values.
Results may differ from the reference program's by a relative error of at most 0.000055.
Values sent between devices are 32-bit elements; how exact they have to be, the bound alone decides.
No kernel may reach another device: no remote copies, remote signals or barrier semaphores. Data moves between devices by JAX's collectives and lax.ppermute only.
A program may use at most 32 MiB of HBM per device.

```python
import math
import jax
import jax.numpy as jnp
from jax import lax

N = 512
ROWS = 262144


def draw_spectra(key, part):
    keys = [jax.random.fold_in(key, 11 + number) for number in range(5)]
    column_scale = 0.5 * jnp.exp(jax.random.uniform(keys[1], (1, N), jnp.float32) * math.log(2.0))
    row_scale = 0.25 * jnp.exp(jax.random.uniform(keys[2], (ROWS, 1), jnp.float32) * math.log(10.0))
    trend = jnp.exp(jnp.arange(ROWS, dtype=jnp.float32)[:, None] * (math.log(3.0) / ROWS))
    common = jnp.clip(jax.random.normal(keys[3], (ROWS, 1), jnp.float32), -4.0, 4.0)
    base = jnp.clip(jax.random.normal(keys[0], (ROWS, N), jnp.float32), -6.0, 6.0)
    weights = jax.random.uniform(keys[4], (1, N), jnp.float32, 0.5, 1.5)
    mixed = 0.3 * common * weights + base
    return mixed * column_scale * row_scale * trend


def setup_inputs(seed: int = 0) -> dict:
    key_list = jax.random.split(jax.random.key(seed), 2)
    spectra = draw_spectra(jax.random.fold_in(key_list[1], 71), 0)
    return dict(spectra=spectra)


def reference(spectra):
    gram = lax.dot_general(spectra.astype(jnp.float32), spectra.astype(jnp.float32), (((0,), (0,)), ((), ())), precision=lax.Precision.HIGHEST, preferred_element_type=jnp.float32)
    lower = jnp.linalg.cholesky(gram)
    basis = lax.linalg.triangular_solve(lower, spectra, left_side=False, lower=True, transpose_a=True)
    factor_scale = math.sqrt(ROWS)
    return (basis * factor_scale, lower.T / factor_scale)
```

```python
import math

import jax
import jax.numpy as jnp
from jax import lax
from jax.sharding import PartitionSpec as P

AXES = ("rows", "chip")


def local_gram(block):
    return lax.dot_general(
        block,
        block,
        (((0,), (0,)), ((), ())),
        precision=lax.Precision.HIGHEST,
        preferred_element_type=jnp.float32,
    )


def summed(gram):
    n_dev = lax.axis_size("rows") * lax.axis_size("chip")
    steps = int(math.log2(n_dev))
    assert 1 << steps == n_dev
    me = lax.axis_index(AXES)
    shape = gram.shape
    x = gram.reshape(-1, 128)
    masks = [1 << k for k in range(steps)]
    for m in masks:
        half = x.shape[0] // 2
        bit = (me // m) % 2
        keep = lax.dynamic_slice_in_dim(x, bit * half, half, 0)
        send = lax.dynamic_slice_in_dim(x, (1 - bit) * half, half, 0)
        perm = [(i, i ^ m) for i in range(n_dev)]
        x = keep + lax.ppermute(send, AXES, perm)
    for m in reversed(masks):
        bit = (me // m) % 2
        perm = [(i, i ^ m) for i in range(n_dev)]
        other = lax.ppermute(x, AXES, perm)
        lo = jnp.where(bit == 0, x, other)
        hi = jnp.where(bit == 0, other, x)
        x = jnp.concatenate([lo, hi], axis=0)
    return x.reshape(shape)


def on_device(spectra):
    total_rows = lax.axis_size("rows") * lax.axis_size("chip") * spectra.shape[0]
    lower = jnp.linalg.cholesky(summed(local_gram(spectra)))
    basis = lax.linalg.triangular_solve(
        lower, spectra, left_side=False, lower=True, transpose_a=True
    )
    factor_scale = math.sqrt(total_rows)
    return (basis * factor_scale, lower.T / factor_scale)


def solution(mesh):
    return jax.shard_map(
        on_device,
        mesh=mesh,
        in_specs=(P(AXES, None),),
        out_specs=(P(AXES, None), P()),
        check_vma=False,
    )
```

```python
import math

import jax
import jax.numpy as jnp
from jax import lax
from jax.sharding import PartitionSpec as P

AXES = ("rows", "chip")


def local_gram(block):
    return lax.dot_general(
        block,
        block,
        (((0,), (0,)), ((), ())),
        precision=lax.Precision.HIGHEST,
        preferred_element_type=jnp.float32,
    )


def groups_of(n_dev):
    bits = int(math.log2(n_dev))
    assert 1 << bits == n_dev
    fields, lo = [(0, 1)], 1
    while lo < bits:
        width = min(3, bits - lo)
        fields.append((lo, width))
        lo += width
    return fields


def member(index, lo, width, sub):
    k = 1 << width
    return index - (((index >> lo) % k) << lo) + (sub << lo)


def summed(gram):
    n_dev = lax.axis_size("rows") * lax.axis_size("chip")
    me = lax.axis_index(AXES)
    shape = gram.shape
    x = gram.reshape(-1, 128)
    fields = groups_of(n_dev)
    for lo, width in fields:
        k = 1 << width
        g = (me >> lo) % k
        part = x.shape[0] // k
        total = lax.dynamic_slice_in_dim(x, g * part, part, 0)
        for s in range(1, k):
            perm = [(i, member(i, lo, width, (((i >> lo) % k) + s) % k)) for i in range(n_dev)]
            send = lax.dynamic_slice_in_dim(x, ((g + s) % k) * part, part, 0)
            total = total + lax.ppermute(send, AXES, perm)
        x = total
    for lo, width in reversed(fields):
        k = 1 << width
        g = (me >> lo) % k
        out = jnp.zeros((k * x.shape[0], 128), x.dtype)
        out = lax.dynamic_update_slice_in_dim(out, x, g * x.shape[0], 0)
        for s in range(1, k):
            perm = [(i, member(i, lo, width, (((i >> lo) % k) + s) % k)) for i in range(n_dev)]
            got = lax.ppermute(x, AXES, perm)
            out = lax.dynamic_update_slice_in_dim(out, got, ((g - s) % k) * x.shape[0], 0)
        x = out
    return x.reshape(shape)


def on_device(spectra):
    total_rows = lax.axis_size("rows") * lax.axis_size("chip") * spectra.shape[0]
    lower = jnp.linalg.cholesky(summed(local_gram(spectra)))
    basis = lax.linalg.triangular_solve(
        lower, spectra, left_side=False, lower=True, transpose_a=True
    )
    factor_scale = math.sqrt(total_rows)
    return (basis * factor_scale, lower.T / factor_scale)


def solution(mesh):
    return jax.shard_map(
        on_device,
        mesh=mesh,
        in_specs=(P(AXES, None),),
        out_specs=(P(AXES, None), P()),
        check_vma=False,
    )
```

```python
import math

import jax
import jax.numpy as jnp
from jax import lax
from jax.sharding import PartitionSpec as P

AXES = ("rows", "chip")
BLOCK = 128


def mm(a, b, dims):
    return lax.dot_general(
        a, b, (dims, ((), ())), precision=lax.Precision.HIGHEST, preferred_element_type=jnp.float32
    )


def summed(gram):
    n_dev = lax.axis_size("rows") * lax.axis_size("chip")
    steps = int(math.log2(n_dev))
    assert 1 << steps == n_dev
    me = lax.axis_index(AXES)
    shape = gram.shape
    x = gram.reshape(-1, 128)
    masks = [1 << k for k in range(steps)]
    for m in masks:
        half = x.shape[0] // 2
        bit = (me // m) % 2
        keep = lax.dynamic_slice_in_dim(x, bit * half, half, 0)
        send = lax.dynamic_slice_in_dim(x, (1 - bit) * half, half, 0)
        perm = [(i, i ^ m) for i in range(n_dev)]
        x = keep + lax.ppermute(send, AXES, perm)
    for m in reversed(masks):
        bit = (me // m) % 2
        perm = [(i, i ^ m) for i in range(n_dev)]
        other = lax.ppermute(x, AXES, perm)
        lo = jnp.where(bit == 0, x, other)
        hi = jnp.where(bit == 0, other, x)
        x = jnp.concatenate([lo, hi], axis=0)
    return x.reshape(shape)


def factor(gram):
    a = (gram + gram.T) / 2
    n = a.shape[0]
    nb = n // BLOCK
    cols, invs = [], []
    for j in range(nb):
        s = slice(j * BLOCK, (j + 1) * BLOCK)
        rest = a[j * BLOCK:, s]
        if j:
            done = jnp.concatenate([c[j * BLOCK - k * BLOCK:] for k, c in enumerate(cols)], axis=1)
            rest = rest - mm(done, done[:BLOCK], ((1,), (1,)))
        diag = lax.linalg.cholesky(rest[:BLOCK], symmetrize_input=False)
        inv = lax.linalg.triangular_solve(
            diag, jnp.eye(BLOCK, dtype=diag.dtype), left_side=True, lower=True
        )
        col = diag
        if j < nb - 1:
            col = jnp.concatenate([diag, mm(rest[BLOCK:], inv, ((1,), (1,)))], axis=0)
        cols.append(col)
        invs.append(inv)
    lower = jnp.concatenate(
        [jnp.concatenate([jnp.zeros((k * BLOCK, BLOCK), a.dtype), c], axis=0) for k, c in enumerate(cols)],
        axis=1,
    )
    return lower, invs


def whiten(spectra, lower, invs):
    outs = []
    for j, inv in enumerate(invs):
        rhs = spectra[:, j * BLOCK:(j + 1) * BLOCK]
        if j:
            prev = jnp.concatenate(outs, axis=1)
            rhs = rhs - mm(prev, lower[j * BLOCK:(j + 1) * BLOCK, : j * BLOCK], ((1,), (1,)))
        outs.append(mm(rhs, inv, ((1,), (1,))))
    return jnp.concatenate(outs, axis=1)


def on_device(spectra):
    total_rows = lax.axis_size("rows") * lax.axis_size("chip") * spectra.shape[0]
    gram = summed(mm(spectra, spectra, ((0,), (0,))))
    lower, invs = factor(gram)
    basis = whiten(spectra, lower, invs)
    factor_scale = math.sqrt(total_rows)
    return (basis * factor_scale, lower.T / factor_scale)


def solution(mesh):
    return jax.shard_map(
        on_device,
        mesh=mesh,
        in_specs=(P(AXES, None),),
        out_specs=(P(AXES, None), P()),
        check_vma=False,
    )
```

```python
import math

import jax
import jax.numpy as jnp
from jax import lax
from jax.sharding import PartitionSpec as P

AXES = ("rows", "chip")
BLOCK = 128


def mm(a, b, dims):
    return lax.dot_general(
        a, b, (dims, ((), ())), precision=lax.Precision.HIGHEST, preferred_element_type=jnp.float32
    )


def summed(gram):
    n_chip = lax.axis_size("chip")
    n_rows = lax.axis_size("rows")
    steps = int(math.log2(n_chip))
    assert 1 << steps == n_chip
    me = lax.axis_index("chip")
    shape = gram.shape
    x = gram.reshape(-1, 128)
    masks = [1 << k for k in range(steps)]
    for m in masks:
        half = x.shape[0] // 2
        bit = (me // m) % 2
        keep = lax.dynamic_slice_in_dim(x, bit * half, half, 0)
        send = lax.dynamic_slice_in_dim(x, (1 - bit) * half, half, 0)
        perm = [(i, i ^ m) for i in range(n_chip)]
        x = keep + lax.ppermute(send, "chip", perm)
    part = x.shape[0] // n_rows
    got = lax.all_to_all(x, "rows", 0, 0, tiled=True)
    x = jnp.sum(got.reshape(n_rows, part, 128), axis=0)
    x = lax.all_to_all(jnp.tile(x, (n_rows, 1)), "rows", 0, 0, tiled=True)
    for m in reversed(masks):
        bit = (me // m) % 2
        perm = [(i, i ^ m) for i in range(n_chip)]
        other = lax.ppermute(x, "chip", perm)
        lo = jnp.where(bit == 0, x, other)
        hi = jnp.where(bit == 0, other, x)
        x = jnp.concatenate([lo, hi], axis=0)
    return x.reshape(shape)


def factor(gram):
    a = (gram + gram.T) / 2
    n = a.shape[0]
    nb = n // BLOCK
    cols, invs = [], []
    for j in range(nb):
        s = slice(j * BLOCK, (j + 1) * BLOCK)
        rest = a[j * BLOCK:, s]
        if j:
            done = jnp.concatenate([c[j * BLOCK - k * BLOCK:] for k, c in enumerate(cols)], axis=1)
            rest = rest - mm(done, done[:BLOCK], ((1,), (1,)))
        diag = lax.linalg.cholesky(rest[:BLOCK], symmetrize_input=False)
        inv = lax.linalg.triangular_solve(
            diag, jnp.eye(BLOCK, dtype=diag.dtype), left_side=True, lower=True
        )
        col = diag
        if j < nb - 1:
            col = jnp.concatenate([diag, mm(rest[BLOCK:], inv, ((1,), (1,)))], axis=0)
        cols.append(col)
        invs.append(inv)
    lower = jnp.concatenate(
        [jnp.concatenate([jnp.zeros((k * BLOCK, BLOCK), a.dtype), c], axis=0) for k, c in enumerate(cols)],
        axis=1,
    )
    return lower, invs


def whiten(spectra, lower, invs):
    outs = []
    for j, inv in enumerate(invs):
        rhs = spectra[:, j * BLOCK:(j + 1) * BLOCK]
        if j:
            prev = jnp.concatenate(outs, axis=1)
            rhs = rhs - mm(prev, lower[j * BLOCK:(j + 1) * BLOCK, : j * BLOCK], ((1,), (1,)))
        outs.append(mm(rhs, inv, ((1,), (1,))))
    return jnp.concatenate(outs, axis=1)


def on_device(spectra):
    total_rows = lax.axis_size("rows") * lax.axis_size("chip") * spectra.shape[0]
    gram = summed(mm(spectra, spectra, ((0,), (0,))))
    lower, invs = factor(gram)
    basis = whiten(spectra, lower, invs)
    factor_scale = math.sqrt(total_rows)
    return (basis * factor_scale, lower.T / factor_scale)


def solution(mesh):
    return jax.shard_map(
        on_device,
        mesh=mesh,
        in_specs=(P(AXES, None),),
        out_specs=(P(AXES, None), P()),
        check_vma=False,
    )
```

```python
import math

import jax
import jax.numpy as jnp
from jax import lax
from jax.sharding import PartitionSpec as P

AXES = ("rows", "chip")
BLOCK = 128


def mm(a, b, dims):
    return lax.dot_general(
        a, b, (dims, ((), ())), precision=lax.Precision.HIGHEST, preferred_element_type=jnp.float32
    )


def summed(gram):
    n_rows = lax.axis_size("rows")
    n_chip = lax.axis_size("chip")
    shape = gram.shape
    x = gram.reshape(-1, 128)
    for axis, n in (("rows", n_rows), ("chip", n_chip)):
        got = lax.all_to_all(x, axis, 0, 0, tiled=True)
        x = jnp.sum(got.reshape(n, x.shape[0] // n, 128), axis=0)
    for axis, n in (("chip", n_chip), ("rows", n_rows)):
        x = lax.all_to_all(jnp.tile(x, (n, 1)), axis, 0, 0, tiled=True)
    return x.reshape(shape)


def factor(gram):
    a = (gram + gram.T) / 2
    n = a.shape[0]
    nb = n // BLOCK
    cols, invs = [], []
    for j in range(nb):
        s = slice(j * BLOCK, (j + 1) * BLOCK)
        rest = a[j * BLOCK:, s]
        if j:
            done = jnp.concatenate([c[j * BLOCK - k * BLOCK:] for k, c in enumerate(cols)], axis=1)
            rest = rest - mm(done, done[:BLOCK], ((1,), (1,)))
        diag = lax.linalg.cholesky(rest[:BLOCK], symmetrize_input=False)
        inv = lax.linalg.triangular_solve(
            diag, jnp.eye(BLOCK, dtype=diag.dtype), left_side=True, lower=True
        )
        col = diag
        if j < nb - 1:
            col = jnp.concatenate([diag, mm(rest[BLOCK:], inv, ((1,), (1,)))], axis=0)
        cols.append(col)
        invs.append(inv)
    lower = jnp.concatenate(
        [jnp.concatenate([jnp.zeros((k * BLOCK, BLOCK), a.dtype), c], axis=0) for k, c in enumerate(cols)],
        axis=1,
    )
    return lower, invs


def whiten(spectra, lower, invs):
    outs = []
    for j, inv in enumerate(invs):
        rhs = spectra[:, j * BLOCK:(j + 1) * BLOCK]
        if j:
            prev = jnp.concatenate(outs, axis=1)
            rhs = rhs - mm(prev, lower[j * BLOCK:(j + 1) * BLOCK, : j * BLOCK], ((1,), (1,)))
        outs.append(mm(rhs, inv, ((1,), (1,))))
    return jnp.concatenate(outs, axis=1)


def on_device(spectra):
    total_rows = lax.axis_size("rows") * lax.axis_size("chip") * spectra.shape[0]
    gram = summed(mm(spectra, spectra, ((0,), (0,))))
    lower, invs = factor(gram)
    basis = whiten(spectra, lower, invs)
    factor_scale = math.sqrt(total_rows)
    return (basis * factor_scale, lower.T / factor_scale)


def solution(mesh):
    return jax.shard_map(
        on_device,
        mesh=mesh,
        in_specs=(P(AXES, None),),
        out_specs=(P(AXES, None), P()),
        check_vma=False,
    )
```

```python
import math

import jax
import jax.numpy as jnp
from jax import lax
from jax.sharding import PartitionSpec as P

AXES = ("rows", "chip")
BLOCK = 128


def mm(a, b, dims):
    return lax.dot_general(
        a, b, (dims, ((), ())), precision=lax.Precision.HIGHEST, preferred_element_type=jnp.float32
    )


def lower_pairs(nb):
    return [(i, j) for j in range(nb) for i in range(j, nb)]


def summed(packed):
    n_rows = lax.axis_size("rows")
    n_chip = lax.axis_size("chip")
    x = packed
    got = lax.all_to_all(x, "rows", 0, 0, tiled=True)
    x = jnp.sum(got.reshape(n_rows, x.shape[0] // n_rows, BLOCK), axis=0)
    kept = x.shape[0]
    padded = -(-kept // n_chip) * n_chip
    x = jnp.pad(x, ((0, padded - kept), (0, 0)))
    got = lax.all_to_all(x, "chip", 0, 0, tiled=True)
    x = jnp.sum(got.reshape(n_chip, padded // n_chip, BLOCK), axis=0)
    x = lax.all_to_all(jnp.tile(x, (n_chip, 1)), "chip", 0, 0, tiled=True)[:kept]
    return lax.all_to_all(jnp.tile(x, (n_rows, 1)), "rows", 0, 0, tiled=True)


def factor(blocks, nb):
    cols, invs = [], []
    for j in range(nb):
        diag = blocks[(j, j)]
        rest = jnp.concatenate([(diag + diag.T) / 2] + [blocks[(i, j)] for i in range(j + 1, nb)], axis=0)
        if j:
            done = jnp.concatenate([c[j * BLOCK - k * BLOCK:] for k, c in enumerate(cols)], axis=1)
            rest = rest - mm(done, done[:BLOCK], ((1,), (1,)))
        diag = lax.linalg.cholesky(rest[:BLOCK], symmetrize_input=False)
        inv = lax.linalg.triangular_solve(
            diag, jnp.eye(BLOCK, dtype=diag.dtype), left_side=True, lower=True
        )
        col = diag
        if j < nb - 1:
            col = jnp.concatenate([diag, mm(rest[BLOCK:], inv, ((1,), (1,)))], axis=0)
        cols.append(col)
        invs.append(inv)
    lower = jnp.concatenate(
        [jnp.concatenate([jnp.zeros((k * BLOCK, BLOCK), diag.dtype), c], axis=0) for k, c in enumerate(cols)],
        axis=1,
    )
    return lower, invs


def whiten(spectra, lower, invs):
    outs = []
    for j, inv in enumerate(invs):
        rhs = spectra[:, j * BLOCK:(j + 1) * BLOCK]
        if j:
            prev = jnp.concatenate(outs, axis=1)
            rhs = rhs - mm(prev, lower[j * BLOCK:(j + 1) * BLOCK, : j * BLOCK], ((1,), (1,)))
        outs.append(mm(rhs, inv, ((1,), (1,))))
    return jnp.concatenate(outs, axis=1)


def on_device(spectra):
    total_rows = lax.axis_size("rows") * lax.axis_size("chip") * spectra.shape[0]
    nb = spectra.shape[1] // BLOCK
    pairs = lower_pairs(nb)
    gram = mm(spectra, spectra, ((0,), (0,)))
    packed = jnp.concatenate(
        [gram[i * BLOCK:(i + 1) * BLOCK, j * BLOCK:(j + 1) * BLOCK] for i, j in pairs], axis=0
    )
    total = summed(packed)
    blocks = {p: total[k * BLOCK:(k + 1) * BLOCK] for k, p in enumerate(pairs)}
    lower, invs = factor(blocks, nb)
    basis = whiten(spectra, lower, invs)
    factor_scale = math.sqrt(total_rows)
    return (basis * factor_scale, lower.T / factor_scale)


def solution(mesh):
    return jax.shard_map(
        on_device,
        mesh=mesh,
        in_specs=(P(AXES, None),),
        out_specs=(P(AXES, None), P()),
        check_vma=False,
    )
```

```python
import math

import jax
import jax.numpy as jnp
from jax import lax
from jax.sharding import PartitionSpec as P

AXES = ("rows", "chip")
BLOCK = 128


def mm(a, b, dims):
    return lax.dot_general(
        a, b, (dims, ((), ())), precision=lax.Precision.HIGHEST, preferred_element_type=jnp.float32
    )


def lower_pairs(nb):
    return [(i, j) for j in range(nb) for i in range(j, nb)]


def summed(packed):
    n_rows = lax.axis_size("rows")
    n_chip = lax.axis_size("chip")
    x = packed
    got = lax.all_to_all(x, "rows", 0, 0, tiled=True)
    x = jnp.sum(got.reshape(n_rows, x.shape[0] // n_rows, BLOCK), axis=0)
    got = lax.all_to_all(jnp.tile(x, (n_chip, 1)), "chip", 0, 0, tiled=True)
    x = jnp.sum(got.reshape(n_chip, x.shape[0], BLOCK), axis=0)
    return lax.all_to_all(jnp.tile(x, (n_rows, 1)), "rows", 0, 0, tiled=True)


def factor(blocks, nb):
    cols, invs = [], []
    for j in range(nb):
        diag = blocks[(j, j)]
        rest = jnp.concatenate([(diag + diag.T) / 2] + [blocks[(i, j)] for i in range(j + 1, nb)], axis=0)
        if j:
            done = jnp.concatenate([c[j * BLOCK - k * BLOCK:] for k, c in enumerate(cols)], axis=1)
            rest = rest - mm(done, done[:BLOCK], ((1,), (1,)))
        diag = lax.linalg.cholesky(rest[:BLOCK], symmetrize_input=False)
        inv = lax.linalg.triangular_solve(
            diag, jnp.eye(BLOCK, dtype=diag.dtype), left_side=True, lower=True
        )
        col = diag
        if j < nb - 1:
            col = jnp.concatenate([diag, mm(rest[BLOCK:], inv, ((1,), (1,)))], axis=0)
        cols.append(col)
        invs.append(inv)
    lower = jnp.concatenate(
        [jnp.concatenate([jnp.zeros((k * BLOCK, BLOCK), diag.dtype), c], axis=0) for k, c in enumerate(cols)],
        axis=1,
    )
    return lower, invs


def whiten(spectra, lower, invs):
    outs = []
    for j, inv in enumerate(invs):
        rhs = spectra[:, j * BLOCK:(j + 1) * BLOCK]
        if j:
            prev = jnp.concatenate(outs, axis=1)
            rhs = rhs - mm(prev, lower[j * BLOCK:(j + 1) * BLOCK, : j * BLOCK], ((1,), (1,)))
        outs.append(mm(rhs, inv, ((1,), (1,))))
    return jnp.concatenate(outs, axis=1)


def on_device(spectra):
    total_rows = lax.axis_size("rows") * lax.axis_size("chip") * spectra.shape[0]
    nb = spectra.shape[1] // BLOCK
    pairs = lower_pairs(nb)
    gram = mm(spectra, spectra, ((0,), (0,)))
    packed = jnp.concatenate(
        [gram[i * BLOCK:(i + 1) * BLOCK, j * BLOCK:(j + 1) * BLOCK] for i, j in pairs], axis=0
    )
    total = summed(packed)
    blocks = {p: total[k * BLOCK:(k + 1) * BLOCK] for k, p in enumerate(pairs)}
    lower, invs = factor(blocks, nb)
    basis = whiten(spectra, lower, invs)
    factor_scale = math.sqrt(total_rows)
    return (basis * factor_scale, lower.T / factor_scale)


def solution(mesh):
    return jax.shard_map(
        on_device,
        mesh=mesh,
        in_specs=(P(AXES, None),),
        out_specs=(P(AXES, None), P()),
        check_vma=False,
    )
```

```python
import math

import jax
import jax.numpy as jnp
from jax import lax
from jax.sharding import PartitionSpec as P

AXES = ("rows", "chip")
BLOCK = 128


def mm(a, b, dims):
    return lax.dot_general(
        a, b, (dims, ((), ())), precision=lax.Precision.HIGHEST, preferred_element_type=jnp.float32
    )


def lower_pairs(nb):
    return [(i, j) for j in range(nb) for i in range(j, nb)]


def summed(packed):
    n_rows = lax.axis_size("rows")
    n_chip = lax.axis_size("chip")
    x = packed
    got = lax.all_to_all(x, "rows", 0, 0, tiled=True)
    x = jnp.sum(got.reshape(n_rows, x.shape[0] // n_rows, BLOCK), axis=0)
    got = lax.all_to_all(jnp.tile(x, (n_chip, 1)), "chip", 0, 0, tiled=True)
    x = jnp.sum(got.reshape(n_chip, x.shape[0], BLOCK), axis=0)
    return lax.all_to_all(jnp.tile(x, (n_rows, 1)), "rows", 0, 0, tiled=True)


def factor(blocks, nb):
    cols, invs = [], []
    for j in range(nb):
        diag = blocks[(j, j)]
        rest = jnp.concatenate([(diag + diag.T) / 2] + [blocks[(i, j)] for i in range(j + 1, nb)], axis=0)
        if j:
            done = jnp.concatenate([c[j * BLOCK - k * BLOCK:] for k, c in enumerate(cols)], axis=1)
            rest = rest - mm(done, done[:BLOCK], ((1,), (1,)))
        diag = lax.linalg.cholesky(rest[:BLOCK], symmetrize_input=False)
        inv = lax.linalg.triangular_solve(
            diag, jnp.eye(BLOCK, dtype=diag.dtype), left_side=True, lower=True
        )
        col = diag
        if j < nb - 1:
            col = jnp.concatenate([diag, mm(rest[BLOCK:], inv, ((1,), (1,)))], axis=0)
        cols.append(col)
        invs.append(inv)
    lower = jnp.concatenate(
        [jnp.concatenate([jnp.zeros((k * BLOCK, BLOCK), diag.dtype), c], axis=0) for k, c in enumerate(cols)],
        axis=1,
    )
    return lower, invs


def whiten(spectra, lower, invs):
    outs = []
    for j, inv in enumerate(invs):
        rhs = spectra[:, j * BLOCK:(j + 1) * BLOCK]
        if j:
            prev = jnp.concatenate(outs, axis=1)
            rhs = rhs - mm(prev, lower[j * BLOCK:(j + 1) * BLOCK, : j * BLOCK], ((1,), (1,)))
        outs.append(mm(rhs, inv, ((1,), (1,))))
    return jnp.concatenate(outs, axis=1)


def pack(gram, nb, n_rows):
    blk = lambda i, j: gram[i * BLOCK:(i + 1) * BLOCK, j * BLOCK:(j + 1) * BLOCK]
    parts = [blk(i, j) for j in range(nb) for i in range(j + 1, nb)]
    eye = jnp.eye(BLOCK, dtype=bool)
    low = jnp.tril(jnp.ones((BLOCK, BLOCK), dtype=bool))
    for j in range(0, nb, 2):
        parts.append(jnp.where(low, blk(j, j), blk(j + 1, j + 1)))
    for j in range(0, nb, 2):
        parts.append(jnp.diagonal(blk(j + 1, j + 1))[None, :])
    packed = jnp.concatenate(parts, axis=0)
    rows = packed.shape[0]
    return jnp.pad(packed, ((0, -(-rows // n_rows) * n_rows - rows), (0, 0)))


def unpack(total, nb):
    blocks, k = {}, 0
    for j in range(nb):
        for i in range(j + 1, nb):
            blocks[(i, j)] = total[k * BLOCK:(k + 1) * BLOCK]
            k += 1
    low = jnp.tril(jnp.ones((BLOCK, BLOCK), dtype=bool))
    strict = jnp.tril(jnp.ones((BLOCK, BLOCK), dtype=bool), -1)
    base = k * BLOCK + (nb // 2) * BLOCK
    for n, j in enumerate(range(0, nb, 2)):
        both = total[(k + n) * BLOCK:(k + n + 1) * BLOCK]
        lower = jnp.where(low, both, 0.0)
        blocks[(j, j)] = lower + jnp.where(strict, both, 0.0).T
        upper = jnp.where(strict.T, both, 0.0)
        blocks[(j + 1, j + 1)] = upper + upper.T + jnp.diag(total[base + n])
    return blocks


def on_device(spectra):
    total_rows = lax.axis_size("rows") * lax.axis_size("chip") * spectra.shape[0]
    nb = spectra.shape[1] // BLOCK
    assert nb % 2 == 0
    gram = mm(spectra, spectra, ((0,), (0,)))
    blocks = unpack(summed(pack(gram, nb, lax.axis_size("rows"))), nb)
    lower, invs = factor(blocks, nb)
    basis = whiten(spectra, lower, invs)
    factor_scale = math.sqrt(total_rows)
    return (basis * factor_scale, lower.T / factor_scale)


def solution(mesh):
    return jax.shard_map(
        on_device,
        mesh=mesh,
        in_specs=(P(AXES, None),),
        out_specs=(P(AXES, None), P()),
        check_vma=False,
    )
```

```python
import math

import jax
import jax.numpy as jnp
from jax import lax
from jax.sharding import PartitionSpec as P

AXES = ("rows", "chip")
BLOCK = 128


def mm(a, b, dims):
    return lax.dot_general(
        a, b, (dims, ((), ())), precision=lax.Precision.HIGHEST, preferred_element_type=jnp.float32
    )


def lower_pairs(nb):
    return [(i, j) for j in range(nb) for i in range(j, nb)]


def summed(packed):
    n_rows = lax.axis_size("rows")
    n_chip = lax.axis_size("chip")
    x = packed
    got = lax.all_to_all(x, "rows", 0, 0, tiled=True)
    x = jnp.sum(got.reshape(n_rows, x.shape[0] // n_rows, BLOCK), axis=0)
    got = lax.all_to_all(jnp.tile(x, (n_chip, 1)), "chip", 0, 0, tiled=True)
    x = jnp.sum(got.reshape(n_chip, x.shape[0], BLOCK), axis=0)
    return lax.all_to_all(jnp.tile(x, (n_rows, 1)), "rows", 0, 0, tiled=True)


def factor(blocks, nb):
    cols, invs = [], []
    for j in range(nb):
        diag = blocks[(j, j)]
        rest = jnp.concatenate([(diag + diag.T) / 2] + [blocks[(i, j)] for i in range(j + 1, nb)], axis=0)
        if j:
            done = jnp.concatenate([c[j * BLOCK - k * BLOCK:] for k, c in enumerate(cols)], axis=1)
            rest = rest - mm(done, done[:BLOCK], ((1,), (1,)))
        diag = lax.linalg.cholesky(rest[:BLOCK], symmetrize_input=False)
        inv = lax.linalg.triangular_solve(
            diag, jnp.eye(BLOCK, dtype=diag.dtype), left_side=True, lower=True
        )
        col = diag
        if j < nb - 1:
            col = jnp.concatenate([diag, mm(rest[BLOCK:], inv, ((1,), (1,)))], axis=0)
        cols.append(col)
        invs.append(inv)
    lower = jnp.concatenate(
        [jnp.concatenate([jnp.zeros((k * BLOCK, BLOCK), diag.dtype), c], axis=0) for k, c in enumerate(cols)],
        axis=1,
    )
    return lower, invs


def whiten(spectra, lower, invs):
    outs = []
    for j, inv in enumerate(invs):
        rhs = spectra[:, j * BLOCK:(j + 1) * BLOCK]
        if j:
            prev = jnp.concatenate(outs, axis=1)
            rhs = rhs - mm(prev, lower[j * BLOCK:(j + 1) * BLOCK, : j * BLOCK], ((1,), (1,)))
        outs.append(mm(rhs, inv, ((1,), (1,))))
    return jnp.concatenate(outs, axis=1)


def on_device(spectra):
    total_rows = lax.axis_size("rows") * lax.axis_size("chip") * spectra.shape[0]
    nb = spectra.shape[1] // BLOCK
    pairs = lower_pairs(nb)
    packed = jnp.concatenate(
        [mm(spectra[:, j * BLOCK:], spectra[:, j * BLOCK:(j + 1) * BLOCK], ((0,), (0,))) for j in range(nb)],
        axis=0,
    )
    total = summed(packed)
    blocks = {p: total[k * BLOCK:(k + 1) * BLOCK] for k, p in enumerate(pairs)}
    lower, invs = factor(blocks, nb)
    basis = whiten(spectra, lower, invs)
    factor_scale = math.sqrt(total_rows)
    return (basis * factor_scale, lower.T / factor_scale)


def solution(mesh):
    return jax.shard_map(
        on_device,
        mesh=mesh,
        in_specs=(P(AXES, None),),
        out_specs=(P(AXES, None), P()),
        check_vma=False,
    )
```

```python
import math

import jax
import jax.numpy as jnp
from jax import lax
from jax.sharding import PartitionSpec as P

AXES = ("rows", "chip")
BLOCK = 128


def mm(a, b, dims):
    return lax.dot_general(
        a, b, (dims, ((), ())), precision=lax.Precision.HIGHEST, preferred_element_type=jnp.float32
    )


def lower_pairs(nb):
    return [(i, j) for j in range(nb) for i in range(j, nb)]


def summed(packed):
    n_rows = lax.axis_size("rows")
    n_chip = lax.axis_size("chip")
    x = packed
    got = lax.all_to_all(x, "rows", 0, 0, tiled=True)
    x = jnp.sum(got.reshape(n_rows, x.shape[0] // n_rows, BLOCK), axis=0)
    got = lax.all_to_all(jnp.tile(x, (n_chip, 1)), "chip", 0, 0, tiled=True)
    x = jnp.sum(got.reshape(n_chip, x.shape[0], BLOCK), axis=0)
    return lax.all_to_all(jnp.tile(x, (n_rows, 1)), "rows", 0, 0, tiled=True)


def factor(blocks, nb):
    cols, invs = [], []
    for j in range(nb):
        diag = blocks[(j, j)]
        rest = jnp.concatenate([diag] + [blocks[(i, j)] for i in range(j + 1, nb)], axis=0)
        if j:
            done = jnp.concatenate([c[j * BLOCK - k * BLOCK:] for k, c in enumerate(cols)], axis=1)
            rest = rest - mm(done, done[:BLOCK], ((1,), (1,)))
        diag = lax.linalg.cholesky(rest[:BLOCK], symmetrize_input=False)
        inv = lax.linalg.triangular_solve(
            diag, jnp.eye(BLOCK, dtype=diag.dtype), left_side=True, lower=True
        )
        col = diag
        if j < nb - 1:
            col = jnp.concatenate([diag, mm(rest[BLOCK:], inv, ((1,), (1,)))], axis=0)
        cols.append(col)
        invs.append(inv)
    lower = jnp.concatenate(
        [jnp.concatenate([jnp.zeros((k * BLOCK, BLOCK), diag.dtype), c], axis=0) for k, c in enumerate(cols)],
        axis=1,
    )
    return lower, invs


def whiten(spectra, lower, invs):
    outs = []
    for j, inv in enumerate(invs):
        rhs = spectra[:, j * BLOCK:(j + 1) * BLOCK]
        if j:
            prev = jnp.concatenate(outs, axis=1)
            rhs = rhs - mm(prev, lower[j * BLOCK:(j + 1) * BLOCK, : j * BLOCK], ((1,), (1,)))
        outs.append(mm(rhs, inv, ((1,), (1,))))
    return jnp.concatenate(outs, axis=1)


def on_device(spectra):
    total_rows = lax.axis_size("rows") * lax.axis_size("chip") * spectra.shape[0]
    nb = spectra.shape[1] // BLOCK
    pairs = lower_pairs(nb)
    gram = mm(spectra, spectra, ((0,), (0,)))
    packed = jnp.concatenate(
        [gram[i * BLOCK:(i + 1) * BLOCK, j * BLOCK:(j + 1) * BLOCK] for i, j in pairs], axis=0
    )
    total = summed(packed)
    blocks = {p: total[k * BLOCK:(k + 1) * BLOCK] for k, p in enumerate(pairs)}
    lower, invs = factor(blocks, nb)
    basis = whiten(spectra, lower, invs)
    factor_scale = math.sqrt(total_rows)
    return (basis * factor_scale, lower.T / factor_scale)


def solution(mesh):
    return jax.shard_map(
        on_device,
        mesh=mesh,
        in_specs=(P(AXES, None),),
        out_specs=(P(AXES, None), P()),
        check_vma=False,
    )
```
